256 devices in a mesh: dp: 32 (over z, x), et: 8 (over y, core).
Axes of the slice: x: 4, y: 4, z: 8, core: 2. Of those that a mesh axis runs over, the one named last changes fastest.
Arguments:
- tokens: bfloat16 [4096, 2048], P('dp', 'et'), may hold values from -6 to 6
- cotangent: bfloat16 [4096, 2048], P('dp', 'et'), may hold values from -1.5 to 1.5
- expert_ids: int32 [4096, 8], P('dp'), may hold values from 0 to 63, all different within a row; in each aligned block of 128 rows (0 to 127, 128 to 255, ...) at most 24 rows name the same one
- route_gates: bfloat16 [4096, 8], P('dp'), may hold values from 0.049804688 to 0.3984375
- gate_proj: bfloat16 [64, 2048, 1024], P('dp', None, 'et'), may hold values from -0.125 to 0.125
- up_proj: bfloat16 [64, 2048, 1024], P('dp', None, 'et'), may hold values from -0.125 to 0.125
- down_proj: bfloat16 [64, 1024, 2048], P('dp', 'et'), may hold values from -0.1875 to 0.1875
Outputs:
- mixed: bfloat16 [4096, 2048], P('dp', 'et')
- grad_tokens: bfloat16 [4096, 2048], P('dp', 'et')
- grad_gates: float32 [4096, 8], P('dp')
- grad_gate_proj: float32 [64, 2048, 1024], P('dp', None, 'et')
- grad_up_proj: float32 [64, 2048, 1024], P('dp', None, 'et')
- grad_down_proj: float32 [64, 1024, 2048], P('dp', 'et')
The draws below stay inside these ranges and needn't reach their ends.
Inputs may be any that keep to these rules, and one draw needn't show every extreme that they name: `expert_ids`: each row names 8 different experts. Among the rows of one device (128 aligned rows), no expert is named more than 24 times, a bound that some block reaches.
All inputs are finite; a program needn't handle non-finite values.
Results may differ from the reference program's by a relative error of at most 0.015.
Values may be sent and summed in bfloat16 or wider, within the bound.
No kernel may reach another device: no remote copies, remote signals or barrier semaphores. Data moves between devices by JAX's collectives and lax.ppermute only.
A program may use at most 128 MiB of HBM per device.

```python
import math
import jax
import jax.numpy as jnp
import numpy as np
from jax import lax

D = 2048
FF = 1024
TOP = 8
TOK_DEV = 128
EXPERTS = 64
TOKENS = 4096
CAP = 24
UNITS = 128
N_ET = 8


def level_of(key, shape, cuts, least, top_value):
    factor_of = 1.0
    for dim, blocks in cuts:
        steps = jax.random.uniform(jax.random.fold_in(jax.random.fold_in(key, 6), dim), (blocks,), jnp.float32, least / len(cuts), top_value / len(cuts))
        factor_of = factor_of * jnp.repeat(jnp.exp(steps), shape[dim] // blocks).reshape((-1,) + (1,) * (len(shape) - 1 - dim))
    return factor_of


def shared_out(own_key, own, number, rows, number_of, top, bound, skew):
    sequence = jax.random.permutation(own_key, number_of)
    heavy_load, common = load_shares(number_of, rows * top, bound, skew, True), load_shares(number_of, rows * top, bound, skew, False)
    places = jnp.arange(number_of)

    def named(tallies, turn):
        used = int((tallies > 0).sum())
        fixed = max(1, used // 4)
        moved = fixed + (places - fixed + turn * (used - fixed)) % max(1, number_of - fixed)
        return jnp.zeros((number_of,), jnp.int32).at[sequence[jnp.where(places < fixed, places, moved)]].set(jnp.asarray(tallies, jnp.int32))

    tallies = jnp.where(number % 4 == 0, named(heavy_load, number // 4), named(common, number - number // 4 - 1))
    mixed = jax.random.permutation(jax.random.fold_in(own, 3), number_of)
    giver, sink = mixed[0:number_of // 2 * 2:2], mixed[1:number_of // 2 * 2:2]
    margin = jnp.minimum(tallies[giver] - 1, bound - tallies[sink]) // 2
    margin = jnp.where((giver == sequence[0]) | (sink == sequence[0]) | (tallies[sink] == 0), 0, jnp.maximum(margin, 0))
    moved = jax.random.randint(jax.random.fold_in(own, 4), (number_of // 2,), 0, 1 << 20) % (margin + 1)
    tallies = tallies.at[giver].add(-moved).at[sink].add(moved)
    items = jnp.searchsorted(jnp.cumsum(tallies), jnp.arange(rows * top), side="right").astype(jnp.int32)
    table = items.reshape(top, rows).T
    table = table[jax.random.permutation(jax.random.fold_in(own, 1), rows)]
    turn = jax.random.randint(jax.random.fold_in(own, 2), (rows, 1), 0, top)
    return jnp.take_along_axis(table, (jnp.arange(top)[None, :] + turn) % top, axis=1)


def load_shares(count, total, bound, skew, full):
    portions = [(1 << 20) // math.isqrt(standing ** skew) + 1 for standing in range(1, count + 1)]
    largest = bound if full else min(bound, max(-(-total // count), total * portions[0] // sum(portions)))
    least = 1 if total - largest >= count - 1 else 0
    counts, surplus = [largest] + [least] * (count - 1), total - largest - least * (count - 1)
    while surplus > 0:
        movable = [i for i in range(1, count) if counts[i] < largest] or [i for i in range(1, count) if counts[i] < bound]
        pool, left = sum([portions[i] for i in movable]), surplus
        for i in movable:
            extra = min(bound - counts[i], max(1, left * portions[i] // pool), surplus)
            counts[i] = counts[i] + extra
            surplus = surplus - extra
    return np.array(counts)


def scatter_about(key, shape, deviation, reach, shards=(), held_as=jnp.bfloat16):
    result = deviation * jax.random.normal(key, shape, jnp.float32)
    if shards:
        result = result * level_of(key, shape, shards, -0.22, 0.18)
    return jnp.clip(result, -reach, reach).astype(held_as)


def setup_inputs(seed: int = 0) -> dict:
    streams_of = jax.random.split(jax.random.key(seed), 8)
    tokens = scatter_about(streams_of[0], (TOKENS, D), 1.0, 6.0, ((0, 32), (1, 8)))
    cotangent = scatter_about(streams_of[1], (TOKENS, D), 0.25, 1.5, ((0, 32), (1, 8)))
    expert_ids_keys = jax.random.split(jax.random.fold_in(streams_of[2], 1), TOKENS // TOK_DEV)
    expert_ids_turns = jax.random.permutation(jax.random.fold_in(streams_of[2], 3), TOKENS // TOK_DEV)
    expert_ids = jax.vmap(lambda own, number: shared_out(jax.random.fold_in(streams_of[2], 2), own, number, TOK_DEV, EXPERTS, TOP, CAP, 2))(expert_ids_keys, expert_ids_turns).reshape((TOKENS, TOP))
    route_gates = jnp.clip(0.049804688 + 0.3486328 * jax.random.uniform(streams_of[3], (TOKENS, TOP), jnp.float32) ** level_of(streams_of[3], (TOKENS, TOP), ((0, 32),), -0.2, 0.2), 0.049804688, 0.3984375).astype(jnp.bfloat16)
    gate_proj = scatter_about(streams_of[4], (EXPERTS, D, FF), D ** -0.5, 0.125, ((0, 32), (2, 8)))
    up_proj = scatter_about(streams_of[5], (EXPERTS, D, FF), D ** -0.5, 0.125, ((0, 32), (2, 8)))
    down_proj = scatter_about(streams_of[6], (EXPERTS, FF, D), FF ** -0.5, 0.1875, ((0, 32), (1, 8)))
    return dict(tokens=tokens, cotangent=cotangent, expert_ids=expert_ids, route_gates=route_gates, gate_proj=gate_proj, up_proj=up_proj, down_proj=down_proj)


def places_in_block(chosen, experts):
    flattened = chosen.reshape(-1)
    onehot = (flattened[:, None] == jnp.arange(experts, dtype=jnp.int32)[None, :]).astype(jnp.int32)
    before = jnp.cumsum(onehot, axis=0) - onehot
    return jnp.sum(before * onehot, axis=1).astype(jnp.int32)


def reference(tokens, cotangent, expert_ids, route_gates, gate_proj, up_proj, down_proj):
    blocks = TOKENS // TOK_DEV
    assignments = TOKENS * TOP
    slot_span = blocks * CAP
    places = jax.vmap(lambda c: places_in_block(c, EXPERTS))(expert_ids.reshape(blocks, TOK_DEV, TOP)).reshape(-1)
    flattened = expert_ids.reshape(-1)
    source = (jnp.arange(assignments, dtype=jnp.int32) // (TOK_DEV * TOP)).astype(jnp.int32)
    slot_index = (flattened * slot_span + source * CAP + places).astype(jnp.int32)
    lookup = jnp.full((EXPERTS * slot_span,), assignments, jnp.int32).at[slot_index].set(jnp.arange(assignments, dtype=jnp.int32))
    lookup = lookup.reshape(EXPERTS, slot_span)
    tokens_ext = jnp.concatenate([tokens, jnp.zeros((1, D), jnp.bfloat16)], axis=0)
    cotangent_ext = jnp.concatenate([cotangent, jnp.zeros((1, D), jnp.bfloat16)], axis=0)
    gates_ext = jnp.concatenate([route_gates.reshape(-1).astype(jnp.float32), jnp.zeros((1,), jnp.float32)], axis=0)

    def per_expert(operands):
        rows_lookup, gate_matrix, up_matrix, down_matrix = operands
        holder = (rows_lookup // TOP).astype(jnp.int32)
        expert_in = tokens_ext[holder]
        expert_cot = (gates_ext[rows_lookup][:, None] * cotangent_ext[holder].astype(jnp.float32)).astype(jnp.bfloat16)
        pre_gate = jnp.dot(expert_in, gate_matrix, preferred_element_type=jnp.float32)
        pre_up = jnp.dot(expert_in, up_matrix, preferred_element_type=jnp.float32)
        sigmoid_gate = jax.nn.sigmoid(pre_gate)
        silu_gate = pre_gate * sigmoid_gate
        hidden = (silu_gate * pre_up).astype(jnp.bfloat16)
        hidden_groups = hidden.reshape(slot_span, N_ET, UNITS).astype(jnp.float32)
        down_groups = down_matrix.reshape(N_ET, UNITS, D).astype(jnp.float32)
        out_parts = jnp.einsum('sjf,jfd->jsd', hidden_groups, down_groups).astype(jnp.bfloat16)
        out_parts = lax.optimization_barrier(out_parts).astype(jnp.float32)
        expert_out = jnp.sum(out_parts, axis=0).astype(jnp.bfloat16)
        grad_hidden = jnp.dot(expert_cot, down_matrix.T, preferred_element_type=jnp.float32)
        grad_pre_gate = (grad_hidden * pre_up * sigmoid_gate * (1.0 + pre_gate * (1.0 - sigmoid_gate))).astype(jnp.bfloat16)
        grad_pre_up = (grad_hidden * silu_gate).astype(jnp.bfloat16)
        grad_down = jnp.dot(hidden.T, expert_cot, preferred_element_type=jnp.float32)
        grad_gate_w = jnp.dot(expert_in.T, grad_pre_gate, preferred_element_type=jnp.float32)
        grad_up_w = jnp.dot(expert_in.T, grad_pre_up, preferred_element_type=jnp.float32)
        gate_groups = gate_matrix.reshape(D, N_ET, UNITS).astype(jnp.float32)
        up_groups = up_matrix.reshape(D, N_ET, UNITS).astype(jnp.float32)
        in_parts = jnp.einsum('sjf,djf->jsd', grad_pre_gate.reshape(slot_span, N_ET, UNITS).astype(jnp.float32), gate_groups)
        in_parts = in_parts + jnp.einsum('sjf,djf->jsd', grad_pre_up.reshape(slot_span, N_ET, UNITS).astype(jnp.float32), up_groups)
        in_parts = lax.optimization_barrier(in_parts.astype(jnp.bfloat16)).astype(jnp.float32)
        grad_in = jnp.sum(in_parts, axis=0).astype(jnp.bfloat16)
        return expert_out, grad_in, grad_gate_w, grad_up_w, grad_down

    expert_out, grad_in, grad_gate_proj, grad_up_proj, grad_down_proj = lax.map(per_expert, (lookup, gate_proj, up_proj, down_proj))
    out_rows = expert_out.reshape(EXPERTS * slot_span, D)[slot_index].reshape(TOKENS, TOP, D).astype(jnp.float32)
    grad_rows = grad_in.reshape(EXPERTS * slot_span, D)[slot_index].reshape(TOKENS, TOP, D).astype(jnp.float32)
    mixed = jnp.sum(route_gates.astype(jnp.float32)[:, :, None] * out_rows, axis=1).astype(jnp.bfloat16)
    grad_gates = jnp.sum(cotangent.astype(jnp.float32)[:, None, :] * out_rows, axis=2)
    grad_tokens = jnp.sum(grad_rows, axis=1).astype(jnp.bfloat16)
    return mixed, grad_tokens, grad_gates, grad_gate_proj, grad_up_proj, grad_down_proj
```

```python
import jax
import jax.numpy as jnp
from jax import lax
from jax.sharding import PartitionSpec as P


def places_in_block(chosen, experts):
    flattened = chosen.reshape(-1)
    pairs = flattened.shape[0]
    onehot = (flattened[:, None] == jnp.arange(experts, dtype=jnp.int32)[None, :]).astype(jnp.bfloat16)
    rows = lax.broadcasted_iota(jnp.int32, (pairs, pairs), 0)
    cols = lax.broadcasted_iota(jnp.int32, (pairs, pairs), 1)
    earlier = (cols < rows).astype(jnp.bfloat16)
    before = jnp.dot(earlier, onehot, preferred_element_type=jnp.float32)
    return jnp.sum(before * onehot.astype(jnp.float32), axis=1).astype(jnp.int32)


def local(tokens, cotangent, expert_ids, route_gates, gate_proj, up_proj, down_proj):
    groups = lax.axis_size("dp")
    shards = lax.axis_size("et")
    local_experts, features, units = gate_proj.shape
    experts = local_experts * groups
    tok_rows, per_token = expert_ids.shape
    width = tokens.shape[1]
    capacity = 3 * tok_rows * per_token // (2 * experts)
    slots = experts * capacity
    places = places_in_block(expert_ids, experts)
    slot_index = (expert_ids.reshape(-1) * capacity + places).reshape(tok_rows, per_token)
    match = slot_index[None, :, :] == jnp.arange(slots, dtype=jnp.int32)[:, None, None]
    select = jnp.any(match, axis=2).astype(jnp.bfloat16)
    gate_select = jnp.sum(
        jnp.where(match, route_gates[None, :, :].astype(jnp.float32), 0.0), axis=2
    ).astype(jnp.bfloat16)
    picked = jnp.dot(select, tokens, preferred_element_type=jnp.float32).astype(jnp.bfloat16)
    scaled = jnp.dot(gate_select, cotangent, preferred_element_type=jnp.float32).astype(
        jnp.bfloat16
    )
    expert_in_part, expert_cot_part = (
        lax.all_to_all(
            picked.reshape(experts, capacity, width), "dp", split_axis=0, concat_axis=1, tiled=True
        ),
        lax.all_to_all(
            scaled.reshape(experts, capacity, width), "dp", split_axis=0, concat_axis=1, tiled=True
        ),
    )
    expert_in = lax.all_gather(expert_in_part, "et", axis=0)
    expert_cot = lax.all_gather(expert_cot_part, "et", axis=0)
    gate_w = gate_proj.reshape(local_experts, shards, width, units)
    up_w = up_proj.reshape(local_experts, shards, width, units)
    down_w = down_proj.reshape(local_experts, units, shards, width)
    pre_gate = jnp.einsum("jesd,ejdf->esf", expert_in, gate_w, preferred_element_type=jnp.float32)
    pre_up = jnp.einsum("jesd,ejdf->esf", expert_in, up_w, preferred_element_type=jnp.float32)
    sigmoid_gate = jax.nn.sigmoid(pre_gate)
    silu_gate = pre_gate * sigmoid_gate
    hidden = (silu_gate * pre_up).astype(jnp.bfloat16)
    out_part = jnp.einsum("esf,efd->esd", hidden, down_proj, preferred_element_type=jnp.float32)
    grad_hidden = jnp.einsum(
        "jesd,efjd->esf", expert_cot, down_w, preferred_element_type=jnp.float32
    )
    grad_pre_gate = (
        grad_hidden * pre_up * sigmoid_gate * (1.0 + pre_gate * (1.0 - sigmoid_gate))
    ).astype(jnp.bfloat16)
    grad_pre_up = (grad_hidden * silu_gate).astype(jnp.bfloat16)
    grad_down = jnp.einsum(
        "esf,jesd->efjd", hidden, expert_cot, preferred_element_type=jnp.float32
    ).reshape(local_experts, units, features)
    grad_gate_w = jnp.einsum(
        "jesd,esf->ejdf", expert_in, grad_pre_gate, preferred_element_type=jnp.float32
    ).reshape(local_experts, features, units)
    grad_up_w = jnp.einsum(
        "jesd,esf->ejdf", expert_in, grad_pre_up, preferred_element_type=jnp.float32
    ).reshape(local_experts, features, units)
    in_part = jnp.einsum(
        "esf,edf->esd", grad_pre_gate, gate_proj, preferred_element_type=jnp.float32
    )
    in_part = in_part + jnp.einsum(
        "esf,edf->esd", grad_pre_up, up_proj, preferred_element_type=jnp.float32
    )
    out_sum, in_sum = (
        lax.psum_scatter(out_part.astype(jnp.bfloat16), "et", scatter_dimension=2, tiled=True),
        lax.psum_scatter(in_part.astype(jnp.bfloat16), "et", scatter_dimension=2, tiled=True),
    )
    back_out, back_grad = (
        lax.all_to_all(out_sum, "dp", split_axis=1, concat_axis=0, tiled=True),
        lax.all_to_all(in_sum, "dp", split_axis=1, concat_axis=0, tiled=True),
    )
    back_out = back_out.reshape(slots, width)
    back_grad = back_grad.reshape(slots, width)
    mixed = jnp.einsum(
        "st,sd->td", gate_select, back_out, preferred_element_type=jnp.float32
    ).astype(jnp.bfloat16)
    grad_tokens = jnp.einsum(
        "st,sd->td", select, back_grad, preferred_element_type=jnp.float32
    ).astype(jnp.bfloat16)
    out_rows = back_out[slot_index.reshape(-1)].reshape(tok_rows, per_token, width).astype(
        jnp.float32
    )
    gate_part = jnp.sum(cotangent.astype(jnp.float32)[:, None, :] * out_rows, axis=2)
    grad_gates = lax.psum(gate_part, "et")
    return (mixed, grad_tokens, grad_gates, grad_gate_w, grad_up_w, grad_down)


def solution(mesh):
    in_specs = (
        P("dp", "et"),
        P("dp", "et"),
        P("dp", None),
        P("dp", None),
        P("dp", None, "et"),
        P("dp", None, "et"),
        P("dp", "et", None),
    )
    out_specs = (
        P("dp", "et"),
        P("dp", "et"),
        P("dp", None),
        P("dp", None, "et"),
        P("dp", None, "et"),
        P("dp", "et", None),
    )
    return jax.shard_map(local, mesh=mesh, in_specs=in_specs, out_specs=out_specs, check_vma=False)
```

```python
import jax
import jax.numpy as jnp
from jax import lax
from jax.sharding import PartitionSpec as P


def places_in_block(chosen, experts):
    flattened = chosen.reshape(-1)
    pairs = flattened.shape[0]
    onehot = (flattened[:, None] == jnp.arange(experts, dtype=jnp.int32)[None, :]).astype(jnp.bfloat16)
    rows = lax.broadcasted_iota(jnp.int32, (pairs, pairs), 0)
    cols = lax.broadcasted_iota(jnp.int32, (pairs, pairs), 1)
    earlier = (cols < rows).astype(jnp.bfloat16)
    before = jnp.dot(earlier, onehot, preferred_element_type=jnp.float32)
    return jnp.sum(before * onehot.astype(jnp.float32), axis=1).astype(jnp.int32)


def local(tokens, cotangent, expert_ids, route_gates, gate_proj, up_proj, down_proj):
    groups = lax.axis_size("dp")
    shards = lax.axis_size("et")
    local_experts, features, units = gate_proj.shape
    experts = local_experts * groups
    tok_rows, per_token = expert_ids.shape
    width = tokens.shape[1]
    capacity = 3 * tok_rows * per_token // (2 * experts)
    slots = experts * capacity
    places = places_in_block(expert_ids, experts)
    slot_index = (expert_ids.reshape(-1) * capacity + places).reshape(tok_rows, per_token)
    by_pair = slot_index.T
    match = by_pair[None, :, :] == jnp.arange(slots, dtype=jnp.int32)[:, None, None]
    select = jnp.any(match, axis=1).astype(jnp.bfloat16)
    gate_select = jnp.sum(
        jnp.where(match, route_gates.T[None, :, :].astype(jnp.float32), 0.0), axis=1
    ).astype(jnp.bfloat16)
    picked = jnp.dot(select, tokens, preferred_element_type=jnp.float32).astype(jnp.bfloat16)
    scaled = jnp.dot(gate_select, cotangent, preferred_element_type=jnp.float32).astype(
        jnp.bfloat16
    )
    routed = jnp.stack([picked, scaled]).reshape(2, experts, capacity, width)
    routed = lax.all_to_all(routed, "dp", split_axis=1, concat_axis=2, tiled=True)
    gathered = lax.all_gather(routed, "et", axis=0)
    expert_in = gathered[:, 0]
    expert_cot = gathered[:, 1]
    gate_w = gate_proj.reshape(local_experts, shards, width, units)
    up_w = up_proj.reshape(local_experts, shards, width, units)
    down_w = down_proj.reshape(local_experts, units, shards, width)
    pre_gate = jnp.einsum("jesd,ejdf->esf", expert_in, gate_w, preferred_element_type=jnp.float32)
    pre_up = jnp.einsum("jesd,ejdf->esf", expert_in, up_w, preferred_element_type=jnp.float32)
    sigmoid_gate = jax.nn.sigmoid(pre_gate)
    silu_gate = pre_gate * sigmoid_gate
    hidden = (silu_gate * pre_up).astype(jnp.bfloat16)
    out_part = jnp.einsum("esf,efd->esd", hidden, down_proj, preferred_element_type=jnp.float32)
    grad_hidden = jnp.einsum(
        "jesd,efjd->esf", expert_cot, down_w, preferred_element_type=jnp.float32
    )
    grad_pre_gate = (
        grad_hidden * pre_up * sigmoid_gate * (1.0 + pre_gate * (1.0 - sigmoid_gate))
    ).astype(jnp.bfloat16)
    grad_pre_up = (grad_hidden * silu_gate).astype(jnp.bfloat16)
    grad_down = jnp.einsum(
        "esf,jesd->efjd", hidden, expert_cot, preferred_element_type=jnp.float32
    ).reshape(local_experts, units, features)
    grad_gate_w = jnp.einsum(
        "jesd,esf->ejdf", expert_in, grad_pre_gate, preferred_element_type=jnp.float32
    ).reshape(local_experts, features, units)
    grad_up_w = jnp.einsum(
        "jesd,esf->ejdf", expert_in, grad_pre_up, preferred_element_type=jnp.float32
    ).reshape(local_experts, features, units)
    in_part = jnp.einsum(
        "esf,edf->esd", grad_pre_gate, gate_proj, preferred_element_type=jnp.float32
    )
    in_part = in_part + jnp.einsum(
        "esf,edf->esd", grad_pre_up, up_proj, preferred_element_type=jnp.float32
    )
    out_sum, in_sum = (
        lax.psum_scatter(out_part.astype(jnp.bfloat16), "et", scatter_dimension=2, tiled=True),
        lax.psum_scatter(in_part.astype(jnp.bfloat16), "et", scatter_dimension=2, tiled=True),
    )
    back_out, back_grad = (
        lax.all_to_all(out_sum, "dp", split_axis=1, concat_axis=0, tiled=True),
        lax.all_to_all(in_sum, "dp", split_axis=1, concat_axis=0, tiled=True),
    )
    back_out = back_out.reshape(slots, width)
    back_grad = back_grad.reshape(slots, width)
    mixed = jnp.einsum(
        "st,sd->td", gate_select, back_out, preferred_element_type=jnp.float32
    ).astype(jnp.bfloat16)
    grad_tokens = jnp.einsum(
        "st,sd->td", select, back_grad, preferred_element_type=jnp.float32
    ).astype(jnp.bfloat16)
    out_rows = back_out[slot_index.reshape(-1)].reshape(tok_rows, per_token, width).astype(
        jnp.float32
    )
    gate_part = jnp.sum(cotangent.astype(jnp.float32)[:, None, :] * out_rows, axis=2)
    grad_gates = lax.psum(gate_part, "et")
    return (mixed, grad_tokens, grad_gates, grad_gate_w, grad_up_w, grad_down)


def solution(mesh):
    in_specs = (
        P("dp", "et"),
        P("dp", "et"),
        P("dp", None),
        P("dp", None),
        P("dp", None, "et"),
        P("dp", None, "et"),
        P("dp", "et", None),
    )
    out_specs = (
        P("dp", "et"),
        P("dp", "et"),
        P("dp", None),
        P("dp", None, "et"),
        P("dp", None, "et"),
        P("dp", "et", None),
    )
    return jax.shard_map(local, mesh=mesh, in_specs=in_specs, out_specs=out_specs, check_vma=False)
```

```python
import jax
import jax.numpy as jnp
from jax import lax
from jax.sharding import PartitionSpec as P


def places_in_block(chosen, experts):
    flattened = chosen.reshape(-1)
    pairs = flattened.shape[0]
    onehot = (flattened[:, None] == jnp.arange(experts, dtype=jnp.int32)[None, :]).astype(jnp.bfloat16)
    rows = lax.broadcasted_iota(jnp.int32, (pairs, pairs), 0)
    cols = lax.broadcasted_iota(jnp.int32, (pairs, pairs), 1)
    earlier = (cols < rows).astype(jnp.bfloat16)
    before = jnp.dot(earlier, onehot, preferred_element_type=jnp.float32)
    return jnp.sum(before * onehot.astype(jnp.float32), axis=1).astype(jnp.int32)


def local(tokens, cotangent, expert_ids, route_gates, gate_proj, up_proj, down_proj):
    groups = lax.axis_size("dp")
    shards = lax.axis_size("et")
    local_experts, features, units = gate_proj.shape
    experts = local_experts * groups
    tok_rows, per_token = expert_ids.shape
    width = tokens.shape[1]
    capacity = 3 * tok_rows * per_token // (2 * experts)
    slots = experts * capacity
    places = places_in_block(expert_ids, experts)
    slot_index = (expert_ids.reshape(-1) * capacity + places).reshape(tok_rows, per_token)
    pairs = tok_rows * per_token
    pair_slot = (
        slot_index.reshape(pairs, 1) == jnp.arange(slots, dtype=jnp.int32)[None, :]
    ).astype(jnp.bfloat16)
    owner = (
        lax.broadcasted_iota(jnp.int32, (tok_rows, pairs), 1) // per_token
        == lax.broadcasted_iota(jnp.int32, (tok_rows, pairs), 0)
    )
    gate_owner = jnp.where(owner, route_gates.reshape(1, pairs), jnp.zeros((), jnp.bfloat16))
    select = jnp.einsum(
        "tp,ps->st", owner.astype(jnp.bfloat16), pair_slot, preferred_element_type=jnp.float32
    ).astype(jnp.bfloat16)
    gate_select = jnp.einsum(
        "tp,ps->st", gate_owner, pair_slot, preferred_element_type=jnp.float32
    ).astype(jnp.bfloat16)
    picked = jnp.dot(select, tokens, preferred_element_type=jnp.float32).astype(jnp.bfloat16)
    scaled = jnp.dot(gate_select, cotangent, preferred_element_type=jnp.float32).astype(
        jnp.bfloat16
    )
    expert_in_part, expert_cot_part = (
        lax.all_to_all(
            picked.reshape(experts, capacity, width), "dp", split_axis=0, concat_axis=1, tiled=True
        ),
        lax.all_to_all(
            scaled.reshape(experts, capacity, width), "dp", split_axis=0, concat_axis=1, tiled=True
        ),
    )
    expert_in = lax.all_gather(expert_in_part, "et", axis=0)
    expert_cot = lax.all_gather(expert_cot_part, "et", axis=0)
    gate_w = gate_proj.reshape(local_experts, shards, width, units)
    up_w = up_proj.reshape(local_experts, shards, width, units)
    down_w = down_proj.reshape(local_experts, units, shards, width)
    pre_gate = jnp.einsum("jesd,ejdf->esf", expert_in, gate_w, preferred_element_type=jnp.float32)
    pre_up = jnp.einsum("jesd,ejdf->esf", expert_in, up_w, preferred_element_type=jnp.float32)
    sigmoid_gate = jax.nn.sigmoid(pre_gate)
    silu_gate = pre_gate * sigmoid_gate
    hidden = (silu_gate * pre_up).astype(jnp.bfloat16)
    out_part = jnp.einsum("esf,efd->esd", hidden, down_proj, preferred_element_type=jnp.float32)
    grad_hidden = jnp.einsum(
        "jesd,efjd->esf", expert_cot, down_w, preferred_element_type=jnp.float32
    )
    grad_pre_gate = (
        grad_hidden * pre_up * sigmoid_gate * (1.0 + pre_gate * (1.0 - sigmoid_gate))
    ).astype(jnp.bfloat16)
    grad_pre_up = (grad_hidden * silu_gate).astype(jnp.bfloat16)
    grad_down = jnp.einsum(
        "esf,jesd->efjd", hidden, expert_cot, preferred_element_type=jnp.float32
    ).reshape(local_experts, units, features)
    grad_gate_w = jnp.einsum(
        "jesd,esf->ejdf", expert_in, grad_pre_gate, preferred_element_type=jnp.float32
    ).reshape(local_experts, features, units)
    grad_up_w = jnp.einsum(
        "jesd,esf->ejdf", expert_in, grad_pre_up, preferred_element_type=jnp.float32
    ).reshape(local_experts, features, units)
    in_part = jnp.einsum(
        "esf,edf->esd", grad_pre_gate, gate_proj, preferred_element_type=jnp.float32
    )
    in_part = in_part + jnp.einsum(
        "esf,edf->esd", grad_pre_up, up_proj, preferred_element_type=jnp.float32
    )
    out_sum = lax.psum_scatter(
        out_part.astype(jnp.bfloat16), "et", scatter_dimension=2, tiled=True
    )
    in_part, grad_gate_w, grad_up_w, grad_down = lax.optimization_barrier(
        (in_part.astype(jnp.bfloat16), grad_gate_w, grad_up_w, grad_down)
    )
    in_sum = lax.psum_scatter(in_part, "et", scatter_dimension=2, tiled=True)
    back_out, back_grad = (
        lax.all_to_all(out_sum, "dp", split_axis=1, concat_axis=0, tiled=True),
        lax.all_to_all(in_sum, "dp", split_axis=1, concat_axis=0, tiled=True),
    )
    back_out = back_out.reshape(slots, width)
    back_grad = back_grad.reshape(slots, width)
    mixed = jnp.einsum(
        "st,sd->td", gate_select, back_out, preferred_element_type=jnp.float32
    ).astype(jnp.bfloat16)
    grad_tokens = jnp.einsum(
        "st,sd->td", select, back_grad, preferred_element_type=jnp.float32
    ).astype(jnp.bfloat16)
    out_rows = back_out[slot_index.reshape(-1)].reshape(tok_rows, per_token, width).astype(
        jnp.float32
    )
    gate_part = jnp.sum(cotangent.astype(jnp.float32)[:, None, :] * out_rows, axis=2)
    grad_gates = lax.psum(gate_part, "et")
    return (mixed, grad_tokens, grad_gates, grad_gate_w, grad_up_w, grad_down)


def solution(mesh):
    in_specs = (
        P("dp", "et"),
        P("dp", "et"),
        P("dp", None),
        P("dp", None),
        P("dp", None, "et"),
        P("dp", None, "et"),
        P("dp", "et", None),
    )
    out_specs = (
        P("dp", "et"),
        P("dp", "et"),
        P("dp", None),
        P("dp", None, "et"),
        P("dp", None, "et"),
        P("dp", "et", None),
    )
    return jax.shard_map(local, mesh=mesh, in_specs=in_specs, out_specs=out_specs, check_vma=False)
```

```python
import jax
import jax.numpy as jnp
from jax import lax
from jax.sharding import PartitionSpec as P


def places_in_block(chosen, experts):
    flattened = chosen.reshape(-1)
    pairs = flattened.shape[0]
    onehot = (flattened[:, None] == jnp.arange(experts, dtype=jnp.int32)[None, :]).astype(jnp.bfloat16)
    rows = lax.broadcasted_iota(jnp.int32, (pairs, pairs), 0)
    cols = lax.broadcasted_iota(jnp.int32, (pairs, pairs), 1)
    earlier = (cols < rows).astype(jnp.bfloat16)
    before = jnp.dot(earlier, onehot, preferred_element_type=jnp.float32)
    return jnp.sum(before * onehot.astype(jnp.float32), axis=1).astype(jnp.int32)


def layer(tokens, cotangent, expert_ids, route_gates, gate_proj, up_proj, down_proj):
    groups = lax.axis_size("dp")
    shards = lax.axis_size("et")
    local_experts, features, units = gate_proj.shape
    experts = local_experts * groups
    tok_rows, per_token = expert_ids.shape
    width = tokens.shape[1]
    capacity = 3 * tok_rows * per_token // (2 * experts)
    slots = experts * capacity
    places = places_in_block(expert_ids, experts)
    slot_index = (expert_ids.reshape(-1) * capacity + places).reshape(tok_rows, per_token)
    pairs = tok_rows * per_token
    pair_slot = (
        slot_index.reshape(pairs, 1) == jnp.arange(slots, dtype=jnp.int32)[None, :]
    ).astype(jnp.bfloat16)
    owner = (
        lax.broadcasted_iota(jnp.int32, (tok_rows, pairs), 1) // per_token
        == lax.broadcasted_iota(jnp.int32, (tok_rows, pairs), 0)
    )
    gate_owner = jnp.where(owner, route_gates.reshape(1, pairs), jnp.zeros((), jnp.bfloat16))
    select = jnp.einsum(
        "tp,ps->st", owner.astype(jnp.bfloat16), pair_slot, preferred_element_type=jnp.float32
    ).astype(jnp.bfloat16)
    gate_select = jnp.einsum(
        "tp,ps->st", gate_owner, pair_slot, preferred_element_type=jnp.float32
    ).astype(jnp.bfloat16)
    picked = jnp.dot(select, tokens, preferred_element_type=jnp.float32).astype(jnp.bfloat16)
    scaled = jnp.dot(gate_select, cotangent, preferred_element_type=jnp.float32).astype(
        jnp.bfloat16
    )
    expert_in_part, expert_cot_part = (
        lax.all_to_all(
            picked.reshape(experts, capacity, width), "dp", split_axis=0, concat_axis=1, tiled=True
        ),
        lax.all_to_all(
            scaled.reshape(experts, capacity, width), "dp", split_axis=0, concat_axis=1, tiled=True
        ),
    )
    expert_in = lax.all_gather(expert_in_part, "et", axis=0)
    expert_cot = lax.all_gather(expert_cot_part, "et", axis=0)
    gate_w = gate_proj.reshape(local_experts, shards, width, units)
    up_w = up_proj.reshape(local_experts, shards, width, units)
    down_w = down_proj.reshape(local_experts, units, shards, width)
    pre_gate = jnp.einsum("jesd,ejdf->esf", expert_in, gate_w, preferred_element_type=jnp.float32)
    pre_up = jnp.einsum("jesd,ejdf->esf", expert_in, up_w, preferred_element_type=jnp.float32)
    sigmoid_gate = jax.nn.sigmoid(pre_gate)
    silu_gate = pre_gate * sigmoid_gate
    hidden = (silu_gate * pre_up).astype(jnp.bfloat16)
    out_part = jnp.einsum(
        "esf,efd->esd", hidden, down_proj, preferred_element_type=jnp.float32
    ).astype(jnp.bfloat16)
    pre_gate, pre_up, hidden = lax.optimization_barrier((pre_gate, pre_up, hidden))
    sigmoid_gate = jax.nn.sigmoid(pre_gate)
    silu_gate = pre_gate * sigmoid_gate
    grad_hidden = jnp.einsum(
        "jesd,efjd->esf", expert_cot, down_w, preferred_element_type=jnp.float32
    )
    grad_pre_gate = (
        grad_hidden * pre_up * sigmoid_gate * (1.0 + pre_gate * (1.0 - sigmoid_gate))
    ).astype(jnp.bfloat16)
    grad_pre_up = (grad_hidden * silu_gate).astype(jnp.bfloat16)
    grad_down = jnp.einsum(
        "esf,jesd->efjd", hidden, expert_cot, preferred_element_type=jnp.float32
    ).reshape(local_experts, units, features)
    grad_gate_w = jnp.einsum(
        "jesd,esf->ejdf", expert_in, grad_pre_gate, preferred_element_type=jnp.float32
    ).reshape(local_experts, features, units)
    grad_up_w = jnp.einsum(
        "jesd,esf->ejdf", expert_in, grad_pre_up, preferred_element_type=jnp.float32
    ).reshape(local_experts, features, units)
    in_part = jnp.einsum(
        "esf,edf->esd", grad_pre_gate, gate_proj, preferred_element_type=jnp.float32
    )
    in_part = in_part + jnp.einsum(
        "esf,edf->esd", grad_pre_up, up_proj, preferred_element_type=jnp.float32
    )
    out_sum = lax.psum_scatter(
        out_part, "et", scatter_dimension=2, tiled=True
    )
    in_part, grad_gate_w, grad_up_w, grad_down = lax.optimization_barrier(
        (in_part.astype(jnp.bfloat16), grad_gate_w, grad_up_w, grad_down)
    )
    in_sum = lax.psum_scatter(in_part, "et", scatter_dimension=2, tiled=True)
    back_out, back_grad = (
        lax.all_to_all(out_sum, "dp", split_axis=1, concat_axis=0, tiled=True),
        lax.all_to_all(in_sum, "dp", split_axis=1, concat_axis=0, tiled=True),
    )
    back_out = back_out.reshape(slots, width)
    back_grad = back_grad.reshape(slots, width)
    mixed = jnp.einsum(
        "st,sd->td", gate_select, back_out, preferred_element_type=jnp.float32
    ).astype(jnp.bfloat16)
    grad_tokens = jnp.einsum(
        "st,sd->td", select, back_grad, preferred_element_type=jnp.float32
    ).astype(jnp.bfloat16)
    out_rows = back_out[slot_index.reshape(-1)].reshape(tok_rows, per_token, width).astype(
        jnp.float32
    )
    gate_part = jnp.sum(cotangent.astype(jnp.float32)[:, None, :] * out_rows, axis=2)
    grad_gates = lax.psum(gate_part, "et")
    return (mixed, grad_tokens, grad_gates, grad_gate_w, grad_up_w, grad_down)


def solution(mesh):
    in_specs = (
        P("dp", "et"),
        P("dp", "et"),
        P("dp", None),
        P("dp", None),
        P("dp", None, "et"),
        P("dp", None, "et"),
        P("dp", "et", None),
    )
    out_specs = (
        P("dp", "et"),
        P("dp", "et"),
        P("dp", None),
        P("dp", None, "et"),
        P("dp", None, "et"),
        P("dp", "et", None),
    )
    return jax.shard_map(layer, mesh=mesh, in_specs=in_specs, out_specs=out_specs, check_vma=False)
```

```python
import jax
import jax.numpy as jnp
from jax import lax
from jax.sharding import PartitionSpec as P


def places_in_block(chosen, experts):
    flattened = chosen.reshape(-1)
    pairs = flattened.shape[0]
    onehot = (flattened[:, None] == jnp.arange(experts, dtype=jnp.int32)[None, :]).astype(jnp.bfloat16)
    rows = lax.broadcasted_iota(jnp.int32, (pairs, pairs), 0)
    cols = lax.broadcasted_iota(jnp.int32, (pairs, pairs), 1)
    earlier = (cols < rows).astype(jnp.bfloat16)
    before = jnp.dot(earlier, onehot, preferred_element_type=jnp.float32)
    return jnp.sum(before * onehot.astype(jnp.float32), axis=1).astype(jnp.int32)


def layer(tokens, cotangent, expert_ids, route_gates, gate_proj, up_proj, down_proj):
    groups = lax.axis_size("dp")
    shards = lax.axis_size("et")
    local_experts, features, units = gate_proj.shape
    experts = local_experts * groups
    tok_rows, per_token = expert_ids.shape
    width = tokens.shape[1]
    capacity = 3 * tok_rows * per_token // (2 * experts)
    slots = experts * capacity
    places = places_in_block(expert_ids, experts)
    slot_index = (expert_ids.reshape(-1) * capacity + places).reshape(tok_rows, per_token)
    pairs = tok_rows * per_token
    pair_slot = (
        slot_index.reshape(pairs, 1) == jnp.arange(slots, dtype=jnp.int32)[None, :]
    ).astype(jnp.bfloat16)
    owner = (
        lax.broadcasted_iota(jnp.int32, (tok_rows, pairs), 1) // per_token
        == lax.broadcasted_iota(jnp.int32, (tok_rows, pairs), 0)
    )
    gate_owner = jnp.where(owner, route_gates.reshape(1, pairs), jnp.zeros((), jnp.bfloat16))
    select = jnp.einsum(
        "tp,ps->st", owner.astype(jnp.bfloat16), pair_slot, preferred_element_type=jnp.float32
    ).astype(jnp.bfloat16)
    gate_select = jnp.einsum(
        "tp,ps->st", gate_owner, pair_slot, preferred_element_type=jnp.float32
    ).astype(jnp.bfloat16)
    picked = jnp.dot(select, tokens, preferred_element_type=jnp.float32).astype(jnp.bfloat16)
    scaled = jnp.dot(gate_select, cotangent, preferred_element_type=jnp.float32).astype(
        jnp.bfloat16
    )
    expert_in_part, expert_cot_part = (
        lax.all_to_all(
            picked.reshape(experts, capacity, width), "dp", split_axis=0, concat_axis=1, tiled=True
        ),
        lax.all_to_all(
            scaled.reshape(experts, capacity, width), "dp", split_axis=0, concat_axis=1, tiled=True
        ),
    )
    expert_in = lax.all_gather(expert_in_part, "et", axis=0)
    expert_cot = lax.all_gather(expert_cot_part, "et", axis=0)
    gate_w = gate_proj.reshape(local_experts, shards, width, units)
    up_w = up_proj.reshape(local_experts, shards, width, units)
    down_w = down_proj.reshape(local_experts, units, shards, width)
    pre_gate = jnp.einsum("jesd,ejdf->esf", expert_in, gate_w, preferred_element_type=jnp.float32)
    pre_up = jnp.einsum("jesd,ejdf->esf", expert_in, up_w, preferred_element_type=jnp.float32)
    sigmoid_gate = jax.nn.sigmoid(pre_gate)
    silu_gate = pre_gate * sigmoid_gate
    hidden = (silu_gate * pre_up).astype(jnp.bfloat16)
    out_part = jnp.einsum(
        "esf,efd->esd", hidden, down_proj, preferred_element_type=jnp.float32
    ).astype(jnp.bfloat16)
    pre_gate, pre_up, hidden = lax.optimization_barrier((pre_gate, pre_up, hidden))
    sigmoid_gate = jax.nn.sigmoid(pre_gate)
    silu_gate = pre_gate * sigmoid_gate
    grad_hidden = jnp.einsum(
        "jesd,efjd->esf", expert_cot, down_w, preferred_element_type=jnp.float32
    )
    grad_pre_gate = (
        grad_hidden * pre_up * sigmoid_gate * (1.0 + pre_gate * (1.0 - sigmoid_gate))
    ).astype(jnp.bfloat16)
    grad_pre_up = (grad_hidden * silu_gate).astype(jnp.bfloat16)
    grad_down = jnp.einsum(
        "esf,jesd->efjd", hidden, expert_cot, preferred_element_type=jnp.float32
    ).reshape(local_experts, units, features)
    grad_gate_w = jnp.einsum(
        "jesd,esf->ejdf", expert_in, grad_pre_gate, preferred_element_type=jnp.float32
    ).reshape(local_experts, features, units)
    grad_up_w = jnp.einsum(
        "jesd,esf->ejdf", expert_in, grad_pre_up, preferred_element_type=jnp.float32
    ).reshape(local_experts, features, units)
    in_part = jnp.einsum(
        "esf,edf->esd", grad_pre_gate, gate_proj, preferred_element_type=jnp.float32
    )
    in_part = in_part + jnp.einsum(
        "esf,edf->esd", grad_pre_up, up_proj, preferred_element_type=jnp.float32
    )
    out_sum = lax.psum_scatter(
        out_part, "et", scatter_dimension=2, tiled=True
    )
    in_part, grad_gate_w, grad_up_w, grad_down = lax.optimization_barrier(
        (in_part.astype(jnp.bfloat16), grad_gate_w, grad_up_w, grad_down)
    )
    in_sum = lax.psum_scatter(in_part, "et", scatter_dimension=2, tiled=True)
    back_out = lax.all_to_all(out_sum, "dp", split_axis=1, concat_axis=0, tiled=True)
    back_grad = lax.all_to_all(in_sum, "dp", split_axis=1, concat_axis=0, tiled=True)
    back_out = back_out.reshape(slots, width)
    back_grad = back_grad.reshape(slots, width)
    mixed = jnp.einsum(
        "st,sd->td", gate_select, back_out, preferred_element_type=jnp.float32
    ).astype(jnp.bfloat16)
    grad_tokens = jnp.einsum(
        "st,sd->td", select, back_grad, preferred_element_type=jnp.float32
    ).astype(jnp.bfloat16)
    out_rows = back_out[slot_index.reshape(-1)].reshape(tok_rows, per_token, width).astype(
        jnp.float32
    )
    gate_part = jnp.sum(cotangent.astype(jnp.float32)[:, None, :] * out_rows, axis=2)
    grad_gates = lax.psum(gate_part, "et")
    return (mixed, grad_tokens, grad_gates, grad_gate_w, grad_up_w, grad_down)


def solution(mesh):
    in_specs = (
        P("dp", "et"),
        P("dp", "et"),
        P("dp", None),
        P("dp", None),
        P("dp", None, "et"),
        P("dp", None, "et"),
        P("dp", "et", None),
    )
    out_specs = (
        P("dp", "et"),
        P("dp", "et"),
        P("dp", None),
        P("dp", None, "et"),
        P("dp", None, "et"),
        P("dp", "et", None),
    )
    return jax.shard_map(layer, mesh=mesh, in_specs=in_specs, out_specs=out_specs, check_vma=False)
```

```python
import jax
import jax.numpy as jnp
from jax import lax
from jax.sharding import PartitionSpec as P


def places_in_block(chosen, experts):
    flattened = chosen.reshape(-1)
    pairs = flattened.shape[0]
    onehot = (flattened[:, None] == jnp.arange(experts, dtype=jnp.int32)[None, :]).astype(jnp.bfloat16)
    rows = lax.broadcasted_iota(jnp.int32, (pairs, pairs), 0)
    cols = lax.broadcasted_iota(jnp.int32, (pairs, pairs), 1)
    earlier = (cols < rows).astype(jnp.bfloat16)
    before = jnp.dot(earlier, onehot, preferred_element_type=jnp.float32)
    return jnp.sum(before * onehot.astype(jnp.float32), axis=1).astype(jnp.int32)


def layer(tokens, cotangent, expert_ids, route_gates, gate_proj, up_proj, down_proj):
    groups = lax.axis_size("dp")
    shards = lax.axis_size("et")
    local_experts, features, units = gate_proj.shape
    experts = local_experts * groups
    tok_rows, per_token = expert_ids.shape
    width = tokens.shape[1]
    capacity = 3 * tok_rows * per_token // (2 * experts)
    slots = experts * capacity
    places = places_in_block(expert_ids, experts)
    slot_index = (expert_ids.reshape(-1) * capacity + places).reshape(tok_rows, per_token)
    pairs = tok_rows * per_token
    pair_slot = (
        slot_index.reshape(pairs, 1) == jnp.arange(slots, dtype=jnp.int32)[None, :]
    ).astype(jnp.bfloat16)
    owner = (
        lax.broadcasted_iota(jnp.int32, (tok_rows, pairs), 1) // per_token
        == lax.broadcasted_iota(jnp.int32, (tok_rows, pairs), 0)
    )
    gate_owner = jnp.where(owner, route_gates.reshape(1, pairs), jnp.zeros((), jnp.bfloat16))
    select = jnp.einsum(
        "tp,ps->st", owner.astype(jnp.bfloat16), pair_slot, preferred_element_type=jnp.float32
    ).astype(jnp.bfloat16)
    gate_select = jnp.einsum(
        "tp,ps->st", gate_owner, pair_slot, preferred_element_type=jnp.float32
    ).astype(jnp.bfloat16)
    picked = jnp.dot(select, tokens, preferred_element_type=jnp.float32).astype(jnp.bfloat16)
    scaled = jnp.dot(gate_select, cotangent, preferred_element_type=jnp.float32).astype(
        jnp.bfloat16
    )
    expert_in_part, expert_cot_part = (
        lax.all_to_all(
            picked.reshape(experts, capacity, width), "dp", split_axis=0, concat_axis=1, tiled=True
        ),
        lax.all_to_all(
            scaled.reshape(experts, capacity, width), "dp", split_axis=0, concat_axis=1, tiled=True
        ),
    )
    expert_in = lax.all_gather(expert_in_part, "et", axis=0)
    expert_cot = lax.all_gather(expert_cot_part, "et", axis=0)
    gate_w = gate_proj.reshape(local_experts, shards, width, units)
    up_w = up_proj.reshape(local_experts, shards, width, units)
    down_w = down_proj.reshape(local_experts, units, shards, width)
    pre_gate = jnp.einsum("jesd,ejdf->esf", expert_in, gate_w, preferred_element_type=jnp.float32)
    pre_up = jnp.einsum("jesd,ejdf->esf", expert_in, up_w, preferred_element_type=jnp.float32)
    sigmoid_gate = jax.nn.sigmoid(pre_gate)
    silu_gate = pre_gate * sigmoid_gate
    hidden = (silu_gate * pre_up).astype(jnp.bfloat16)
    out_part = jnp.einsum(
        "esf,efd->esd", hidden, down_proj, preferred_element_type=jnp.float32
    ).astype(jnp.bfloat16)
    pre_gate, pre_up, hidden = lax.optimization_barrier((pre_gate, pre_up, hidden))
    sigmoid_gate = jax.nn.sigmoid(pre_gate)
    silu_gate = pre_gate * sigmoid_gate
    grad_hidden = jnp.einsum(
        "jesd,efjd->esf", expert_cot, down_w, preferred_element_type=jnp.float32
    )
    grad_pre_gate = (
        grad_hidden * pre_up * sigmoid_gate * (1.0 + pre_gate * (1.0 - sigmoid_gate))
    ).astype(jnp.bfloat16)
    grad_pre_up = (grad_hidden * silu_gate).astype(jnp.bfloat16)
    grad_down = jnp.einsum(
        "esf,jesd->efjd", hidden, expert_cot, preferred_element_type=jnp.float32
    ).reshape(local_experts, units, features)
    grad_gate_w = jnp.einsum(
        "jesd,esf->ejdf", expert_in, grad_pre_gate, preferred_element_type=jnp.float32
    ).reshape(local_experts, features, units)
    grad_up_w = jnp.einsum(
        "jesd,esf->ejdf", expert_in, grad_pre_up, preferred_element_type=jnp.float32
    ).reshape(local_experts, features, units)
    in_part = jnp.einsum(
        "esf,edf->esd", grad_pre_gate, gate_proj, preferred_element_type=jnp.float32
    )
    in_part = in_part + jnp.einsum(
        "esf,edf->esd", grad_pre_up, up_proj, preferred_element_type=jnp.float32
    )
    out_sum = lax.psum_scatter(
        out_part, "et", scatter_dimension=2, tiled=True
    )
    in_part, grad_gate_w, grad_up_w, grad_down = lax.optimization_barrier(
        (in_part.astype(jnp.bfloat16), grad_gate_w, grad_up_w, grad_down)
    )
    in_sum = lax.psum_scatter(in_part, "et", scatter_dimension=2, tiled=True)
    back_out = lax.all_to_all(out_sum, "dp", split_axis=1, concat_axis=0, tiled=True)
    back_grad = lax.all_to_all(in_sum, "dp", split_axis=1, concat_axis=0, tiled=True)
    back_out = back_out.reshape(slots, width)
    back_grad = back_grad.reshape(slots, width)
    mixed = jnp.einsum(
        "st,sd->td", gate_select, back_out, preferred_element_type=jnp.float32
    ).astype(jnp.bfloat16)
    grad_tokens = jnp.einsum(
        "st,sd->td", select, back_grad, preferred_element_type=jnp.float32
    ).astype(jnp.bfloat16)
    out_rows = back_out[slot_index.reshape(-1)].reshape(tok_rows, per_token, width).astype(
        jnp.float32
    )
    gate_part = jnp.sum(cotangent.astype(jnp.float32)[:, None, :] * out_rows, axis=2)
    grad_gates = gate_part
    step = 1
    while step < shards:
        swap = [(i, i ^ step) for i in range(shards)]
        grad_gates = grad_gates + lax.ppermute(grad_gates, "et", swap)
        step *= 2
    return (mixed, grad_tokens, grad_gates, grad_gate_w, grad_up_w, grad_down)


def solution(mesh):
    in_specs = (
        P("dp", "et"),
        P("dp", "et"),
        P("dp", None),
        P("dp", None),
        P("dp", None, "et"),
        P("dp", None, "et"),
        P("dp", "et", None),
    )
    out_specs = (
        P("dp", "et"),
        P("dp", "et"),
        P("dp", None),
        P("dp", None, "et"),
        P("dp", None, "et"),
        P("dp", "et", None),
    )
    return jax.shard_map(layer, mesh=mesh, in_specs=in_specs, out_specs=out_specs, check_vma=False)
```

```python
import jax
import jax.numpy as jnp
from jax import lax
from jax.sharding import PartitionSpec as P


def places_in_block(chosen, experts):
    flattened = chosen.reshape(-1)
    pairs = flattened.shape[0]
    onehot = (flattened[:, None] == jnp.arange(experts, dtype=jnp.int32)[None, :]).astype(jnp.bfloat16)
    rows = lax.broadcasted_iota(jnp.int32, (pairs, pairs), 0)
    cols = lax.broadcasted_iota(jnp.int32, (pairs, pairs), 1)
    earlier = (cols < rows).astype(jnp.bfloat16)
    before = jnp.dot(earlier, onehot, preferred_element_type=jnp.float32)
    return jnp.sum(before * onehot.astype(jnp.float32), axis=1).astype(jnp.int32)


def layer(tokens, cotangent, expert_ids, route_gates, gate_proj, up_proj, down_proj):
    groups = lax.axis_size("dp")
    shards = lax.axis_size("et")
    local_experts, features, units = gate_proj.shape
    experts = local_experts * groups
    tok_rows, per_token = expert_ids.shape
    width = tokens.shape[1]
    capacity = 3 * tok_rows * per_token // (2 * experts)
    slots = experts * capacity
    places = places_in_block(expert_ids, experts)
    slot_index = (expert_ids.reshape(-1) * capacity + places).reshape(tok_rows, per_token)
    pairs = tok_rows * per_token
    pair_slot = (
        slot_index.reshape(pairs, 1) == jnp.arange(slots, dtype=jnp.int32)[None, :]
    ).astype(jnp.bfloat16)
    owner = (
        lax.broadcasted_iota(jnp.int32, (tok_rows, pairs), 1) // per_token
        == lax.broadcasted_iota(jnp.int32, (tok_rows, pairs), 0)
    )
    gate_owner = jnp.where(owner, route_gates.reshape(1, pairs), jnp.zeros((), jnp.bfloat16))
    select = jnp.einsum(
        "tp,ps->st", owner.astype(jnp.bfloat16), pair_slot, preferred_element_type=jnp.float32
    ).astype(jnp.bfloat16)
    gate_select = jnp.einsum(
        "tp,ps->st", gate_owner, pair_slot, preferred_element_type=jnp.float32
    ).astype(jnp.bfloat16)
    picked = jnp.dot(select, tokens, preferred_element_type=jnp.float32).astype(jnp.bfloat16)
    scaled = jnp.dot(gate_select, cotangent, preferred_element_type=jnp.float32).astype(
        jnp.bfloat16
    )
    expert_in_part, expert_cot_part = (
        lax.all_to_all(
            picked.reshape(experts, capacity, width), "dp", split_axis=0, concat_axis=1, tiled=True
        ),
        lax.all_to_all(
            scaled.reshape(experts, capacity, width), "dp", split_axis=0, concat_axis=1, tiled=True
        ),
    )
    expert_in = lax.all_gather(expert_in_part, "et", axis=0)
    me = lax.axis_index("et")
    pieces = [expert_cot_part] + [
        lax.ppermute(expert_cot_part, "et", [(i, (i + s) % shards) for i in range(shards)])
        for s in range(1, shards)
    ]
    expert_cot = jnp.take(
        jnp.stack(pieces), (me - jnp.arange(shards)) % shards, axis=0
    )
    gate_w = gate_proj.reshape(local_experts, shards, width, units)
    up_w = up_proj.reshape(local_experts, shards, width, units)
    down_w = down_proj.reshape(local_experts, units, shards, width)
    pre_gate = jnp.einsum("jesd,ejdf->esf", expert_in, gate_w, preferred_element_type=jnp.float32)
    pre_up = jnp.einsum("jesd,ejdf->esf", expert_in, up_w, preferred_element_type=jnp.float32)
    sigmoid_gate = jax.nn.sigmoid(pre_gate)
    silu_gate = pre_gate * sigmoid_gate
    hidden = (silu_gate * pre_up).astype(jnp.bfloat16)
    out_part = jnp.einsum(
        "esf,efd->esd", hidden, down_proj, preferred_element_type=jnp.float32
    ).astype(jnp.bfloat16)
    pre_gate, pre_up, hidden = lax.optimization_barrier((pre_gate, pre_up, hidden))
    sigmoid_gate = jax.nn.sigmoid(pre_gate)
    silu_gate = pre_gate * sigmoid_gate
    grad_hidden = jnp.einsum(
        "jesd,efjd->esf", expert_cot, down_w, preferred_element_type=jnp.float32
    )
    grad_pre_gate = (
        grad_hidden * pre_up * sigmoid_gate * (1.0 + pre_gate * (1.0 - sigmoid_gate))
    ).astype(jnp.bfloat16)
    grad_pre_up = (grad_hidden * silu_gate).astype(jnp.bfloat16)
    grad_down = jnp.einsum(
        "esf,jesd->efjd", hidden, expert_cot, preferred_element_type=jnp.float32
    ).reshape(local_experts, units, features)
    grad_gate_w = jnp.einsum(
        "jesd,esf->ejdf", expert_in, grad_pre_gate, preferred_element_type=jnp.float32
    ).reshape(local_experts, features, units)
    grad_up_w = jnp.einsum(
        "jesd,esf->ejdf", expert_in, grad_pre_up, preferred_element_type=jnp.float32
    ).reshape(local_experts, features, units)
    in_part = jnp.einsum(
        "esf,edf->esd", grad_pre_gate, gate_proj, preferred_element_type=jnp.float32
    )
    in_part = in_part + jnp.einsum(
        "esf,edf->esd", grad_pre_up, up_proj, preferred_element_type=jnp.float32
    )
    out_sum = lax.psum_scatter(
        out_part, "et", scatter_dimension=2, tiled=True
    )
    in_part, grad_gate_w, grad_up_w, grad_down = lax.optimization_barrier(
        (in_part.astype(jnp.bfloat16), grad_gate_w, grad_up_w, grad_down)
    )
    in_sum = lax.psum_scatter(in_part, "et", scatter_dimension=2, tiled=True)
    back_out = lax.all_to_all(out_sum, "dp", split_axis=1, concat_axis=0, tiled=True)
    back_grad = lax.all_to_all(in_sum, "dp", split_axis=1, concat_axis=0, tiled=True)
    back_out = back_out.reshape(slots, width)
    back_grad = back_grad.reshape(slots, width)
    mixed = jnp.einsum(
        "st,sd->td", gate_select, back_out, preferred_element_type=jnp.float32
    ).astype(jnp.bfloat16)
    grad_tokens = jnp.einsum(
        "st,sd->td", select, back_grad, preferred_element_type=jnp.float32
    ).astype(jnp.bfloat16)
    out_rows = back_out[slot_index.reshape(-1)].reshape(tok_rows, per_token, width).astype(
        jnp.float32
    )
    gate_part = jnp.sum(cotangent.astype(jnp.float32)[:, None, :] * out_rows, axis=2)
    grad_gates = gate_part
    step = 1
    while step < shards:
        swap = [(i, i ^ step) for i in range(shards)]
        grad_gates = grad_gates + lax.ppermute(grad_gates, "et", swap)
        step *= 2
    return (mixed, grad_tokens, grad_gates, grad_gate_w, grad_up_w, grad_down)


def solution(mesh):
    in_specs = (
        P("dp", "et"),
        P("dp", "et"),
        P("dp", None),
        P("dp", None),
        P("dp", None, "et"),
        P("dp", None, "et"),
        P("dp", "et", None),
    )
    out_specs = (
        P("dp", "et"),
        P("dp", "et"),
        P("dp", None),
        P("dp", None, "et"),
        P("dp", None, "et"),
        P("dp", "et", None),
    )
    return jax.shard_map(layer, mesh=mesh, in_specs=in_specs, out_specs=out_specs, check_vma=False)
```

```python
import jax
import jax.numpy as jnp
from jax import lax
from jax.sharding import PartitionSpec as P


def places_in_block(chosen, experts):
    flattened = chosen.reshape(-1)
    pairs = flattened.shape[0]
    onehot = (flattened[:, None] == jnp.arange(experts, dtype=jnp.int32)[None, :]).astype(jnp.bfloat16)
    rows = lax.broadcasted_iota(jnp.int32, (pairs, pairs), 0)
    cols = lax.broadcasted_iota(jnp.int32, (pairs, pairs), 1)
    earlier = (cols < rows).astype(jnp.bfloat16)
    before = jnp.dot(earlier, onehot, preferred_element_type=jnp.float32)
    return jnp.sum(before * onehot.astype(jnp.float32), axis=1).astype(jnp.int32)


def layer(tokens, cotangent, expert_ids, route_gates, gate_proj, up_proj, down_proj):
    groups = lax.axis_size("dp")
    shards = lax.axis_size("et")
    local_experts, features, units = gate_proj.shape
    experts = local_experts * groups
    tok_rows, per_token = expert_ids.shape
    width = tokens.shape[1]
    capacity = 3 * tok_rows * per_token // (2 * experts)
    slots = experts * capacity
    places = places_in_block(expert_ids, experts)
    slot_index = (expert_ids.reshape(-1) * capacity + places).reshape(tok_rows, per_token)
    pairs = tok_rows * per_token
    pair_slot = (
        slot_index.reshape(pairs, 1) == jnp.arange(slots, dtype=jnp.int32)[None, :]
    ).astype(jnp.bfloat16)
    owner = (
        lax.broadcasted_iota(jnp.int32, (tok_rows, pairs), 1) // per_token
        == lax.broadcasted_iota(jnp.int32, (tok_rows, pairs), 0)
    )
    gate_owner = jnp.where(owner, route_gates.reshape(1, pairs), jnp.zeros((), jnp.bfloat16))
    select = jnp.einsum(
        "tp,ps->st", owner.astype(jnp.bfloat16), pair_slot, preferred_element_type=jnp.float32
    ).astype(jnp.bfloat16)
    gate_select = jnp.einsum(
        "tp,ps->st", gate_owner, pair_slot, preferred_element_type=jnp.float32
    ).astype(jnp.bfloat16)
    picked = jnp.dot(select, tokens, preferred_element_type=jnp.float32).astype(jnp.bfloat16)
    scaled = jnp.dot(gate_select, cotangent, preferred_element_type=jnp.float32).astype(
        jnp.bfloat16
    )
    expert_in_part, expert_cot_part = (
        lax.all_to_all(
            picked.reshape(experts, capacity, width), "dp", split_axis=0, concat_axis=1, tiled=True
        ),
        lax.all_to_all(
            scaled.reshape(experts, capacity, width), "dp", split_axis=0, concat_axis=1, tiled=True
        ),
    )
    expert_in = lax.all_gather(expert_in_part, "et", axis=0)
    expert_cot = lax.all_gather(expert_cot_part, "et", axis=0)
    gate_w = gate_proj.reshape(local_experts, shards, width, units)
    up_w = up_proj.reshape(local_experts, shards, width, units)
    down_w = down_proj.reshape(local_experts, units, shards, width)
    pre_gate = jnp.einsum("jesd,ejdf->esf", expert_in, gate_w, preferred_element_type=jnp.float32)
    pre_up = jnp.einsum("jesd,ejdf->esf", expert_in, up_w, preferred_element_type=jnp.float32)
    sigmoid_gate = jax.nn.sigmoid(pre_gate)
    silu_gate = pre_gate * sigmoid_gate
    hidden = (silu_gate * pre_up).astype(jnp.bfloat16)
    out_part = jnp.einsum(
        "esf,efd->esd", hidden, down_proj, preferred_element_type=jnp.float32
    ).astype(jnp.bfloat16)
    pre_gate, pre_up, hidden = lax.optimization_barrier((pre_gate, pre_up, hidden))
    sigmoid_gate = jax.nn.sigmoid(pre_gate)
    silu_gate = pre_gate * sigmoid_gate
    grad_hidden = jnp.einsum(
        "jesd,efjd->esf", expert_cot, down_w, preferred_element_type=jnp.float32
    )
    grad_pre_gate = (
        grad_hidden * pre_up * sigmoid_gate * (1.0 + pre_gate * (1.0 - sigmoid_gate))
    ).astype(jnp.bfloat16)
    grad_pre_up = (grad_hidden * silu_gate).astype(jnp.bfloat16)
    grad_down = jnp.einsum(
        "esf,jesd->efjd", hidden, expert_cot, preferred_element_type=jnp.float32
    ).reshape(local_experts, units, features)
    grad_gate_w = jnp.einsum(
        "jesd,esf->ejdf", expert_in, grad_pre_gate, preferred_element_type=jnp.float32
    ).reshape(local_experts, features, units)
    grad_up_w = jnp.einsum(
        "jesd,esf->ejdf", expert_in, grad_pre_up, preferred_element_type=jnp.float32
    ).reshape(local_experts, features, units)
    in_part = jnp.einsum(
        "esf,edf->esd", grad_pre_gate, gate_proj, preferred_element_type=jnp.float32
    )
    in_part = in_part + jnp.einsum(
        "esf,edf->esd", grad_pre_up, up_proj, preferred_element_type=jnp.float32
    )
    out_sum = lax.psum_scatter(
        out_part, "et", scatter_dimension=2, tiled=True
    )
    in_part, grad_gate_w, grad_up_w, grad_down = lax.optimization_barrier(
        (in_part.astype(jnp.bfloat16), grad_gate_w, grad_up_w, grad_down)
    )
    in_part = in_part.reshape(local_experts, groups, capacity, features).transpose(1, 0, 2, 3)
    in_sum = lax.psum_scatter(in_part, "et", scatter_dimension=3, tiled=True)
    back_out = lax.all_to_all(out_sum, "dp", split_axis=1, concat_axis=0, tiled=True)
    back_grad = lax.all_to_all(in_sum, "dp", split_axis=0, concat_axis=0, tiled=True)
    back_out = back_out.reshape(slots, width)
    back_grad = back_grad.reshape(slots, width)
    mixed = jnp.einsum(
        "st,sd->td", gate_select, back_out, preferred_element_type=jnp.float32
    ).astype(jnp.bfloat16)
    grad_tokens = jnp.einsum(
        "st,sd->td", select, back_grad, preferred_element_type=jnp.float32
    ).astype(jnp.bfloat16)
    out_rows = back_out[slot_index.reshape(-1)].reshape(tok_rows, per_token, width).astype(
        jnp.float32
    )
    gate_part = jnp.sum(cotangent.astype(jnp.float32)[:, None, :] * out_rows, axis=2)
    grad_gates = gate_part
    step = 1
    while step < shards:
        swap = [(i, i ^ step) for i in range(shards)]
        grad_gates = grad_gates + lax.ppermute(grad_gates, "et", swap)
        step *= 2
    return (mixed, grad_tokens, grad_gates, grad_gate_w, grad_up_w, grad_down)


def solution(mesh):
    in_specs = (
        P("dp", "et"),
        P("dp", "et"),
        P("dp", None),
        P("dp", None),
        P("dp", None, "et"),
        P("dp", None, "et"),
        P("dp", "et", None),
    )
    out_specs = (
        P("dp", "et"),
        P("dp", "et"),
        P("dp", None),
        P("dp", None, "et"),
        P("dp", None, "et"),
        P("dp", "et", None),
    )
    return jax.shard_map(layer, mesh=mesh, in_specs=in_specs, out_specs=out_specs, check_vma=False)
```
